512 devices in a mesh: dp: 16 (over z, core), mp: 32 (over x, y).
Axes of the slice: x: 4, y: 8, z: 8, core: 2. Of those that a mesh axis runs over, the one named last changes fastest.
Arguments:
- tokens: bfloat16 [2048, 4096], P(('dp', 'mp')), may hold values from -6 to 6
- hidden_grad: bfloat16 [2048, 14336], P('dp', 'mp'), may hold values from -0.125 to 0.125
- gate_weight: bfloat16 [4096, 14336], P('dp', 'mp'), may hold values from -0.09375 to 0.09375
- up_weight: bfloat16 [4096, 14336], P('dp', 'mp'), may hold values from -0.09375 to 0.09375
- gate_probe: bfloat16 [4096, 14336], P('dp', 'mp'), may hold values from -1 to 1, as said below
- gate_mean: float32 [4096, 14336], P('dp', 'mp'), may hold values from -0.6 to 0.6
- gate_curve: float32 [4096, 14336], P('dp', 'mp'), may hold values from 1 to 10
- group_counts: int32 [16], replicated, may hold values from 32 to 128, as said below
Outputs:
- gate_weight_new: bfloat16 [4096, 14336], P('dp', 'mp')
- gate_mean_new: float32 [4096, 14336], P('dp', 'mp')
- gate_curve_new: float32 [4096, 14336], P('dp', 'mp')
The draws below stay inside these ranges and needn't reach their ends.
Inputs may be any that keep to these rules, and one draw needn't show every extreme that they name: `group_counts`: some data group has exactly 128 live tokens in every draw. `gate_probe`: every entry is -1 or 1, each sign drawn independently.
All inputs are finite; a program needn't handle non-finite values.
Results may differ from the reference program's by a relative error of at most 0.0017.
Values may be sent and summed in bfloat16 or wider, within the bound.
No kernel may reach another device: no remote copies, remote signals or barrier semaphores. Data moves between devices by JAX's collectives and lax.ppermute only.
A program may use at most 64 MiB of HBM per device.

```python
import math
import jax
import jax.numpy as jnp
from jax import lax

D = 4096
FF = 14336
GROUP_ROWS = 128
TOKENS = 2048
N_DP = 16


def draw_group_counts(key, part):
    first_key = jax.random.fold_in(key, 11)
    second_key = jax.random.fold_in(key, 12)
    least_rows = max(GROUP_ROWS // 4, 1)
    counts = jax.random.randint(first_key, (N_DP,), least_rows, GROUP_ROWS + 1, dtype=jnp.int32)
    chosen = jax.random.randint(second_key, (), 0, N_DP, dtype=jnp.int32)
    positions = jnp.arange(N_DP, dtype=jnp.int32)
    return jnp.where(positions == chosen, GROUP_ROWS, counts).astype(jnp.int32)


def draw_gate_probe(key, part):
    sign_key = jax.random.fold_in(key, 21)
    signs = jax.random.randint(sign_key, (D, FF), 0, 2, dtype=jnp.int32)
    values = 2.0 * signs.astype(jnp.float32) - 1.0
    return values.astype(jnp.bfloat16)


def block_levels(own_key, dims, shards, least, largest):
    level, own = 1.0, jax.random.fold_in(own_key, 6)
    for dim, blocks in shards:
        steps = jnp.exp(jax.random.uniform(jax.random.fold_in(own, dim), (blocks,), jnp.float32, least / len(shards), largest / len(shards)))
        level = level * jnp.repeat(steps, dims[dim] // blocks).reshape([-1 if axis == dim else 1 for axis in range(len(dims))])
    return level


def normal_values(key, shape, scale, bound, split=(), kind=jnp.bfloat16):
    drawn = scale * jax.random.normal(key, shape, jnp.float32)
    if split:
        drawn = drawn * block_levels(key, shape, split, -0.22, 0.18)
    return jnp.clip(drawn, -bound, bound).astype(kind)


def setup_inputs(seed: int = 0) -> dict:
    key_list = jax.random.split(jax.random.key(seed), 9)
    return {
        "tokens": normal_values(key_list[0], (TOKENS, D), 1.0, 6.0, ((0, 512),)),
        "hidden_grad": normal_values(key_list[1], (TOKENS, FF), TOKENS ** -0.5, 0.125, ((0, 16), (1, 32))),
        "gate_weight": normal_values(key_list[2], (D, FF), D ** -0.5, 0.09375, ((0, 16), (1, 32))),
        "up_weight": normal_values(key_list[3], (D, FF), D ** -0.5, 0.09375, ((0, 16), (1, 32))),
        "gate_probe": draw_gate_probe(jax.random.fold_in(key_list[8], 71), 0),
        "gate_mean": normal_values(key_list[5], (D, FF), 0.1, 0.6, ((0, 16), (1, 32)), jnp.float32),
        "gate_curve": jnp.clip(jnp.exp(math.log(10.0) - 2.3025851 * jax.random.uniform(key_list[6], (D, FF), jnp.float32) ** block_levels(key_list[6], (D, FF), ((0, 16), (1, 32)), -0.2, 0.2)), 1.0, 10.0),
        "group_counts": draw_group_counts(jax.random.fold_in(key_list[8], 71), 0),
    }


first_decay = 0.9
second_decay = 0.999
learn_rate = 0.15
epsilon_term = 0.0001
first_fix = 1.0 - 0.9 ** 10
second_fix = 1.0 - 0.999 ** 10

def silu_parts(inputs):
    sigmoid_part = jax.nn.sigmoid(inputs)
    silu_slope = sigmoid_part * (1.0 + inputs * (1.0 - sigmoid_part))
    silu_bend = sigmoid_part * (1.0 - sigmoid_part) * (2.0 + inputs * (1.0 - 2.0 * sigmoid_part))
    return (silu_slope, silu_bend)

def adahessian(weight, mean_old, curve_old, gradient, probe_value, product):
    diagonal = probe_value.astype(jnp.float32) * product
    mean_new = first_decay * mean_old + (1.0 - first_decay) * gradient
    curve_new = second_decay * curve_old + (1.0 - second_decay) * diagonal * diagonal
    step_ratio = mean_new / first_fix / (jnp.sqrt(curve_new / second_fix) + epsilon_term)
    weight_new = (weight.astype(jnp.float32) - learn_rate * step_ratio).astype(jnp.bfloat16)
    return (weight_new, mean_new, curve_new)

def reference(tokens, hidden_grad, gate_weight, up_weight, gate_probe, gate_mean, gate_curve, group_counts):
    total_rows = tokens.shape[0]
    row_ids = jnp.arange(total_rows, dtype=jnp.int32)
    limits = jnp.repeat(group_counts.astype(jnp.int32), GROUP_ROWS, total_repeat_length=total_rows)
    live = (row_ids % GROUP_ROWS < limits).astype(jnp.float32)

    def project(weight):
        return jnp.dot(tokens, weight, preferred_element_type=jnp.float32)
    gate_pre = project(gate_weight)
    up_pre = project(up_weight)
    gate_tan = project(gate_probe)
    silu_slope, silu_bend = silu_parts(gate_pre)
    masked = hidden_grad.astype(jnp.float32) * live[:, None]
    grad_gate = (masked * up_pre * silu_slope).astype(jnp.bfloat16)
    tan_gate = (masked * up_pre * silu_bend * gate_tan).astype(jnp.bfloat16)

    def contract(rows):
        return lax.dot_general(tokens, rows, (((0,), (0,)), ((), ())), preferred_element_type=jnp.float32)
    gate_gradient = contract(grad_gate)
    gate_hz = contract(tan_gate)
    gate_out = adahessian(gate_weight, gate_mean, gate_curve, gate_gradient, gate_probe, gate_hz)
    return (gate_out[0], gate_out[1], gate_out[2])
```

```python
import jax
import jax.numpy as jnp
from jax import lax
from jax.sharding import PartitionSpec as P

first_decay = 0.9
second_decay = 0.999
learn_rate = 0.15
epsilon_term = 0.0001
first_fix = 1.0 - 0.9**10
second_fix = 1.0 - 0.999**10


def silu_parts(inputs):
    sigmoid_part = jax.nn.sigmoid(inputs)
    silu_slope = sigmoid_part * (1.0 + inputs * (1.0 - sigmoid_part))
    silu_bend = sigmoid_part * (1.0 - sigmoid_part) * (2.0 + inputs * (1.0 - 2.0 * sigmoid_part))
    return (silu_slope, silu_bend)


def adahessian(weight, mean_old, curve_old, gradient, probe_value, product):
    diagonal = probe_value.astype(jnp.float32) * product
    mean_new = first_decay * mean_old + (1.0 - first_decay) * gradient
    curve_new = second_decay * curve_old + (1.0 - second_decay) * diagonal * diagonal
    step_ratio = mean_new / first_fix / (jnp.sqrt(curve_new / second_fix) + epsilon_term)
    weight_new = (weight.astype(jnp.float32) - learn_rate * step_ratio).astype(jnp.bfloat16)
    return (weight_new, mean_new, curve_new)


def chip_ring(x, n_dp):
    n_chip = n_dp // 2
    d = lax.axis_index("dp")
    z = d // 2
    c = d % 2
    rows = x.shape[0]
    partner = [(i, i ^ 1) for i in range(n_dp)]
    ring = [(2 * j, 2 * ((j + 1) % n_chip)) for j in range(n_chip)] + [
        (2 * j + 1, 2 * ((j - 1) % n_chip) + 1) for j in range(n_chip)
    ]
    px = lax.ppermute(x, "dp", partner)
    pieces = [(x, d), (px, d ^ 1)]
    cur = jnp.concatenate([x, px], 0)
    step = 2 * c - 1
    for k in range(1, n_chip // 2 + 1):
        cur = lax.ppermute(cur, "dp", ring)
        j = (z + k * step) % n_chip
        o = c
        pieces.append((cur[:rows], 2 * j + o))
        pieces.append((cur[rows:], 2 * j + 1 - o))
        if k < n_chip // 2:
            ex = lax.ppermute(cur, "dp", partner)
            j2 = (z - k * step) % n_chip
            o2 = 1 - c
            pieces.append((ex[:rows], 2 * j2 + o2))
            pieces.append((ex[rows:], 2 * j2 + 1 - o2))
    return pieces


def body(
    tokens, hidden_grad, gate_weight, up_weight, gate_probe, gate_mean, gate_curve, group_counts
):
    n_dp = lax.axis_size("dp")
    n_mp = lax.axis_size("mp")
    rows_loc, feat = tokens.shape
    shard = feat // n_dp
    width = gate_weight.shape[1]
    d = lax.axis_index("dp")

    t3 = tokens.reshape(rows_loc, n_dp, shard)
    a2a = lax.all_to_all(t3, "dp", split_axis=1, concat_axis=1, tiled=True)
    pack = jnp.concatenate([tokens, a2a.reshape(rows_loc, feat)], 0)
    gathered = lax.all_gather(pack, "mp", axis=0, tiled=False)
    whole = gathered[:, :rows_loc, :].reshape(n_mp * rows_loc, feat)
    group_rows = whole.shape[0]
    cols = (
        gathered[:, rows_loc:, :]
        .reshape(n_mp, rows_loc, n_dp, shard)
        .transpose(2, 0, 1, 3)
        .reshape(n_dp * group_rows, shard)
    )

    w3 = jnp.concatenate([gate_weight, up_weight, gate_probe], 1)
    pre = None
    for piece, s in chip_ring(w3, n_dp):
        part = lax.dynamic_slice_in_dim(whole, s * shard, shard, axis=1)
        term = jnp.dot(part, piece, preferred_element_type=jnp.float32)
        pre = term if pre is None else pre + term
    gate_pre = pre[:, :width]
    up_pre = pre[:, width : 2 * width]
    gate_tan = pre[:, 2 * width :]

    limit = lax.dynamic_index_in_dim(group_counts, d, 0, keepdims=False)
    live = (jnp.arange(group_rows, dtype=jnp.int32) < limit).astype(jnp.float32)
    silu_slope, silu_bend = silu_parts(gate_pre)
    masked = hidden_grad.astype(jnp.float32) * live[:, None]
    grad_gate = (masked * up_pre * silu_slope).astype(jnp.bfloat16)
    tan_gate = (masked * up_pre * silu_bend * gate_tan).astype(jnp.bfloat16)
    packed = jnp.concatenate([grad_gate, tan_gate], 1)

    sums = None
    for piece, g in chip_ring(packed, n_dp):
        part = lax.dynamic_slice_in_dim(cols, g * group_rows, group_rows, axis=0)
        term = lax.dot_general(
            part, piece, (((0,), (0,)), ((), ())), preferred_element_type=jnp.float32
        )
        sums = term if sums is None else sums + term
    gate_out = adahessian(
        gate_weight, gate_mean, gate_curve, sums[:, :width], gate_probe, sums[:, width:]
    )
    return (gate_out[0], gate_out[1], gate_out[2])


def solution(mesh):
    return jax.shard_map(
        body,
        mesh=mesh,
        in_specs=(
            P(("dp", "mp"), None),
            P("dp", "mp"),
            P("dp", "mp"),
            P("dp", "mp"),
            P("dp", "mp"),
            P("dp", "mp"),
            P("dp", "mp"),
            P(),
        ),
        out_specs=(P("dp", "mp"), P("dp", "mp"), P("dp", "mp")),
        check_vma=False,
    )
```

```python
import jax
import jax.numpy as jnp
from jax import lax
from jax.sharding import PartitionSpec as P

first_decay = 0.9
second_decay = 0.999
learn_rate = 0.15
epsilon_term = 0.0001
first_fix = 1.0 - 0.9**10
second_fix = 1.0 - 0.999**10


def silu_parts(inputs):
    sigmoid_part = jax.nn.sigmoid(inputs)
    silu_slope = sigmoid_part * (1.0 + inputs * (1.0 - sigmoid_part))
    silu_bend = sigmoid_part * (1.0 - sigmoid_part) * (2.0 + inputs * (1.0 - 2.0 * sigmoid_part))
    return (silu_slope, silu_bend)


def adahessian(weight, mean_old, curve_old, gradient, probe_value, product):
    diagonal = probe_value.astype(jnp.float32) * product
    mean_new = first_decay * mean_old + (1.0 - first_decay) * gradient
    curve_new = second_decay * curve_old + (1.0 - second_decay) * diagonal * diagonal
    step_ratio = mean_new / first_fix / (jnp.sqrt(curve_new / second_fix) + epsilon_term)
    weight_new = (weight.astype(jnp.float32) - learn_rate * step_ratio).astype(jnp.bfloat16)
    return (weight_new, mean_new, curve_new)


DP = ("z", "c")
MP = ("x", "y")


def chip_ring(x, n_dp):
    n_chip = n_dp // 2
    d = lax.axis_index(DP)
    z = d // 2
    c = d % 2
    rows = x.shape[0]
    partner = [(i, i ^ 1) for i in range(n_dp)]
    ring = [(2 * j, 2 * ((j + 1) % n_chip)) for j in range(n_chip)] + [
        (2 * j + 1, 2 * ((j - 1) % n_chip) + 1) for j in range(n_chip)
    ]
    px = lax.ppermute(x, DP, partner)
    pieces = [(x, d), (px, d ^ 1)]
    cur = jnp.concatenate([x, px], 0)
    step = 2 * c - 1
    for k in range(1, n_chip // 2 + 1):
        cur = lax.ppermute(cur, DP, ring)
        j = (z + k * step) % n_chip
        o = c
        pieces.append((cur[:rows], 2 * j + o))
        pieces.append((cur[rows:], 2 * j + 1 - o))
        if k < n_chip // 2:
            ex = lax.ppermute(cur, DP, partner)
            j2 = (z - k * step) % n_chip
            o2 = 1 - c
            pieces.append((ex[:rows], 2 * j2 + o2))
            pieces.append((ex[rows:], 2 * j2 + 1 - o2))
    return pieces


def body(
    tokens, hidden_grad, gate_weight, up_weight, gate_probe, gate_mean, gate_curve, group_counts
):
    n_dp = lax.axis_size(DP)
    n_mp = lax.axis_size(MP)
    rows_loc, feat = tokens.shape
    shard = feat // n_dp
    width = gate_weight.shape[1]
    d = lax.axis_index(DP)

    def gather_mp(a):
        a = lax.all_gather(a, "y", axis=0, tiled=True)
        return lax.all_gather(a, "x", axis=0, tiled=True)

    whole = gather_mp(tokens)
    group_rows = whole.shape[0]
    t3 = tokens.reshape(rows_loc, n_dp, shard)
    a2a = lax.all_to_all(t3, DP, split_axis=1, concat_axis=1, tiled=True)
    cols = (
        gather_mp(a2a)
        .reshape(n_mp, rows_loc, n_dp, shard)
        .transpose(2, 0, 1, 3)
        .reshape(n_dp * group_rows, shard)
    )

    w3 = jnp.concatenate([gate_weight, up_weight, gate_probe], 1)
    pre = None
    for piece, s in chip_ring(w3, n_dp):
        part = lax.dynamic_slice_in_dim(whole, s * shard, shard, axis=1)
        term = jnp.dot(part, piece, preferred_element_type=jnp.float32)
        pre = term if pre is None else pre + term
    gate_pre = pre[:, :width]
    up_pre = pre[:, width : 2 * width]
    gate_tan = pre[:, 2 * width :]

    limit = lax.dynamic_index_in_dim(group_counts, d, 0, keepdims=False)
    live = (jnp.arange(group_rows, dtype=jnp.int32) < limit).astype(jnp.float32)
    silu_slope, silu_bend = silu_parts(gate_pre)
    masked = hidden_grad.astype(jnp.float32) * live[:, None]
    grad_gate = (masked * up_pre * silu_slope).astype(jnp.bfloat16)
    tan_gate = (masked * up_pre * silu_bend * gate_tan).astype(jnp.bfloat16)
    packed = jnp.concatenate([grad_gate, tan_gate], 1)

    sums = None
    for piece, g in chip_ring(packed, n_dp):
        part = lax.dynamic_slice_in_dim(cols, g * group_rows, group_rows, axis=0)
        term = lax.dot_general(
            part, piece, (((0,), (0,)), ((), ())), preferred_element_type=jnp.float32
        )
        sums = term if sums is None else sums + term
    gate_out = adahessian(
        gate_weight, gate_mean, gate_curve, sums[:, :width], gate_probe, sums[:, width:]
    )
    return (gate_out[0], gate_out[1], gate_out[2])


def solution(mesh):
    n_dp, n_mp = mesh.devices.shape
    n_x = len({dev.coords[0] for dev in mesh.devices[0]})
    mesh4 = jax.sharding.Mesh(
        mesh.devices.reshape(n_dp // 2, 2, n_x, n_mp // n_x), ("z", "c", "x", "y")
    )
    every = DP + MP
    return jax.shard_map(
        body,
        mesh=mesh4,
        in_specs=(
            P(every, None),
            P(DP, MP),
            P(DP, MP),
            P(DP, MP),
            P(DP, MP),
            P(DP, MP),
            P(DP, MP),
            P(),
        ),
        out_specs=(P(DP, MP), P(DP, MP), P(DP, MP)),
        check_vma=False,
    )
```

```python
import jax
import jax.numpy as jnp
from jax import lax
from jax.sharding import PartitionSpec as P


first_decay = 0.9
second_decay = 0.999
learn_rate = 0.15
epsilon_term = 0.0001
first_fix = 1.0 - 0.9**10
second_fix = 1.0 - 0.999**10


def silu_parts(inputs):
    sigmoid_part = jax.nn.sigmoid(inputs)
    silu_slope = sigmoid_part * (1.0 + inputs * (1.0 - sigmoid_part))
    silu_bend = sigmoid_part * (1.0 - sigmoid_part) * (2.0 + inputs * (1.0 - 2.0 * sigmoid_part))
    return (silu_slope, silu_bend)


def adahessian(weight, mean_old, curve_old, gradient, probe_value, product):
    diagonal = probe_value.astype(jnp.float32) * product
    mean_new = first_decay * mean_old + (1.0 - first_decay) * gradient
    curve_new = second_decay * curve_old + (1.0 - second_decay) * diagonal * diagonal
    step_ratio = mean_new / first_fix / (jnp.sqrt(curve_new / second_fix) + epsilon_term)
    weight_new = (weight.astype(jnp.float32) - learn_rate * step_ratio).astype(jnp.bfloat16)
    return (weight_new, mean_new, curve_new)


DP = ("z", "c")
MP = ("x", "y")


def chip_ring(x, n_dp):
    n_chip = n_dp // 2
    d = lax.axis_index(DP)
    z = d // 2
    c = d % 2
    rows = x.shape[0]
    partner = [(i, i ^ 1) for i in range(n_dp)]
    ring = [(2 * j, 2 * ((j + 1) % n_chip)) for j in range(n_chip)] + [
        (2 * j + 1, 2 * ((j - 1) % n_chip) + 1) for j in range(n_chip)
    ]
    px = lax.ppermute(x, DP, partner)
    pieces = [(x, d), (px, d ^ 1)]
    cur = jnp.concatenate([x, px], 0)
    step = 2 * c - 1
    for k in range(1, n_chip // 2 + 1):
        cur = lax.ppermute(cur, DP, ring)
        j = (z + k * step) % n_chip
        o = c
        pieces.append((cur[:rows], 2 * j + o))
        pieces.append((cur[rows:], 2 * j + 1 - o))
        if k < n_chip // 2:
            ex = lax.ppermute(cur, DP, partner)
            j2 = (z - k * step) % n_chip
            o2 = 1 - c
            pieces.append((ex[:rows], 2 * j2 + o2))
            pieces.append((ex[rows:], 2 * j2 + 1 - o2))
    return pieces


def ring_gather(a, name):
    n = lax.axis_size(name)
    idx = lax.axis_index(name)
    fwd = [(i, (i + 1) % n) for i in range(n)]
    bwd = [(i, (i - 1) % n) for i in range(n)]
    n_f = n // 2
    n_b = n - 1 - n_f
    rel = [None] * n
    rel[0] = a
    f = a
    b = a
    for k in range(1, n_f + 1):
        f = lax.ppermute(f, name, fwd)
        rel[n - k] = f
        if k <= n_b:
            b = lax.ppermute(b, name, bwd)
            rel[k] = b
    stacked = jnp.stack(rel, 0)
    ordered = jnp.roll(stacked, idx, axis=0)
    return ordered.reshape((n * a.shape[0],) + a.shape[1:])


def step(
    tokens, hidden_grad, gate_weight, up_weight, gate_probe, gate_mean, gate_curve, group_counts
):
    n_dp = lax.axis_size(DP)
    n_mp = lax.axis_size(MP)
    rows_loc, feat = tokens.shape
    shard = feat // n_dp
    width = gate_weight.shape[1]
    d = lax.axis_index(DP)

    whole = ring_gather(ring_gather(tokens, "y"), "x")
    group_rows = whole.shape[0]
    t3 = tokens.reshape(rows_loc, n_dp, shard)
    a2a = lax.all_to_all(t3, DP, split_axis=1, concat_axis=1, tiled=True)
    cols = (
        lax.all_gather(a2a, MP, axis=0, tiled=True)
        .reshape(n_mp, rows_loc, n_dp, shard)
        .transpose(2, 0, 1, 3)
        .reshape(n_dp * group_rows, shard)
    )

    w3 = jnp.concatenate([gate_weight, up_weight, gate_probe], 1)
    pre = None
    for piece, s in chip_ring(w3, n_dp):
        part = lax.dynamic_slice_in_dim(whole, s * shard, shard, axis=1)
        term = jnp.dot(part, piece, preferred_element_type=jnp.float32)
        pre = term if pre is None else pre + term
    gate_pre = pre[:, :width]
    up_pre = pre[:, width : 2 * width]
    gate_tan = pre[:, 2 * width :]

    limit = lax.dynamic_index_in_dim(group_counts, d, 0, keepdims=False)
    live = (jnp.arange(group_rows, dtype=jnp.int32) < limit).astype(jnp.float32)
    silu_slope, silu_bend = silu_parts(gate_pre)
    masked = hidden_grad.astype(jnp.float32) * live[:, None]
    grad_gate = (masked * up_pre * silu_slope).astype(jnp.bfloat16)
    tan_gate = (masked * up_pre * silu_bend * gate_tan).astype(jnp.bfloat16)
    packed = jnp.concatenate([grad_gate, tan_gate], 1)

    sums = None
    for piece, g in chip_ring(packed, n_dp):
        part = lax.dynamic_slice_in_dim(cols, g * group_rows, group_rows, axis=0)
        term = lax.dot_general(
            part, piece, (((0,), (0,)), ((), ())), preferred_element_type=jnp.float32
        )
        sums = term if sums is None else sums + term
    gate_out = adahessian(
        gate_weight, gate_mean, gate_curve, sums[:, :width], gate_probe, sums[:, width:]
    )
    return (gate_out[0], gate_out[1], gate_out[2])


def solution(mesh):
    n_dp, n_mp = mesh.devices.shape
    n_x = len({dev.coords[0] for dev in mesh.devices[0]})
    mesh4 = jax.sharding.Mesh(
        mesh.devices.reshape(n_dp // 2, 2, n_x, n_mp // n_x), ("z", "c", "x", "y")
    )
    every = DP + MP
    return jax.shard_map(
        step,
        mesh=mesh4,
        in_specs=(
            P(every, None),
            P(DP, MP),
            P(DP, MP),
            P(DP, MP),
            P(DP, MP),
            P(DP, MP),
            P(DP, MP),
            P(),
        ),
        out_specs=(P(DP, MP), P(DP, MP), P(DP, MP)),
        check_vma=False,
    )
```

```python
import jax
import jax.numpy as jnp
from jax import lax
from jax.sharding import PartitionSpec as P


first_decay = 0.9
second_decay = 0.999
learn_rate = 0.15
epsilon_term = 0.0001
first_fix = 1.0 - 0.9**10
second_fix = 1.0 - 0.999**10


def silu_parts(inputs):
    sigmoid_part = jax.nn.sigmoid(inputs)
    silu_slope = sigmoid_part * (1.0 + inputs * (1.0 - sigmoid_part))
    silu_bend = sigmoid_part * (1.0 - sigmoid_part) * (2.0 + inputs * (1.0 - 2.0 * sigmoid_part))
    return (silu_slope, silu_bend)


def adahessian(weight, mean_old, curve_old, gradient, probe_value, product):
    diagonal = probe_value.astype(jnp.float32) * product
    mean_new = first_decay * mean_old + (1.0 - first_decay) * gradient
    curve_new = second_decay * curve_old + (1.0 - second_decay) * diagonal * diagonal
    step_ratio = mean_new / first_fix / (jnp.sqrt(curve_new / second_fix) + epsilon_term)
    weight_new = (weight.astype(jnp.float32) - learn_rate * step_ratio).astype(jnp.bfloat16)
    return (weight_new, mean_new, curve_new)


DP = ("z", "c")
MP = ("x", "y")


def chip_ring(x, n_dp):
    n_chip = n_dp // 2
    d = lax.axis_index(DP)
    z = d // 2
    c = d % 2
    partner = [(i, i ^ 1) for i in range(n_dp)]
    ring = [(2 * j, 2 * ((j + 1) % n_chip)) for j in range(n_chip)] + [
        (2 * j + 1, 2 * ((j - 1) % n_chip) + 1) for j in range(n_chip)
    ]
    px = lax.ppermute(x, DP, partner)
    cur = jnp.concatenate([x, px], 0)
    blocks = [(cur, d, d ^ 1)]
    step = 2 * c - 1
    for k in range(1, n_chip // 2 + 1):
        cur = lax.ppermute(cur, DP, ring)
        j = (z + k * step) % n_chip
        blocks.append((cur, 2 * j + c, 2 * j + 1 - c))
        if k < n_chip // 2:
            ex = lax.ppermute(cur, DP, partner)
            j2 = (z - k * step) % n_chip
            blocks.append((ex, 2 * j2 + 1 - c, 2 * j2 + c))
    return blocks


def step(
    tokens, hidden_grad, gate_weight, up_weight, gate_probe, gate_mean, gate_curve, group_counts
):
    n_dp = lax.axis_size(DP)
    _, feat = tokens.shape
    shard = feat // n_dp
    width = gate_weight.shape[1]
    d = lax.axis_index(DP)

    whole = lax.all_gather(tokens, MP, axis=0, tiled=True)
    group_rows = whole.shape[0]
    cols = lax.all_to_all(whole, DP, split_axis=1, concat_axis=0, tiled=True)

    w3 = jnp.concatenate([gate_weight, up_weight, gate_probe], 1)
    w_full = jnp.zeros((feat, w3.shape[1]), w3.dtype)
    for block, s0, s1 in chip_ring(w3, n_dp):
        w_full = lax.dynamic_update_slice_in_dim(w_full, block[: w3.shape[0]], s0 * shard, 0)
        w_full = lax.dynamic_update_slice_in_dim(w_full, block[w3.shape[0] :], s1 * shard, 0)
    pre = jnp.dot(whole, w_full, preferred_element_type=jnp.float32)
    gate_pre = pre[:, :width]
    up_pre = pre[:, width : 2 * width]
    gate_tan = pre[:, 2 * width :]

    limit = lax.dynamic_index_in_dim(group_counts, d, 0, keepdims=False)
    live = (jnp.arange(group_rows, dtype=jnp.int32) < limit).astype(jnp.float32)
    silu_slope, silu_bend = silu_parts(gate_pre)
    masked = hidden_grad.astype(jnp.float32) * live[:, None]
    grad_gate = (masked * up_pre * silu_slope).astype(jnp.bfloat16)
    tan_gate = (masked * up_pre * silu_bend * gate_tan).astype(jnp.bfloat16)
    packed = jnp.concatenate([grad_gate, tan_gate], 1)

    sums = lax.dot_general(
        cols,
        lax.all_gather(packed, DP, axis=0, tiled=True),
        (((0,), (0,)), ((), ())),
        preferred_element_type=jnp.float32,
    )
    gate_out = adahessian(
        gate_weight, gate_mean, gate_curve, sums[:, :width], gate_probe, sums[:, width:]
    )
    return (gate_out[0], gate_out[1], gate_out[2])


def solution(mesh):
    n_dp, n_mp = mesh.devices.shape
    n_x = len({dev.coords[0] for dev in mesh.devices[0]})
    mesh4 = jax.sharding.Mesh(
        mesh.devices.reshape(n_dp // 2, 2, n_x, n_mp // n_x), ("z", "c", "x", "y")
    )
    every = DP + MP
    return jax.shard_map(
        step,
        mesh=mesh4,
        in_specs=(
            P(every, None),
            P(DP, MP),
            P(DP, MP),
            P(DP, MP),
            P(DP, MP),
            P(DP, MP),
            P(DP, MP),
            P(),
        ),
        out_specs=(P(DP, MP), P(DP, MP), P(DP, MP)),
        check_vma=False,
    )
```

```python
import jax
import jax.numpy as jnp
from jax import lax
from jax.sharding import PartitionSpec as P


first_decay = 0.9
second_decay = 0.999
learn_rate = 0.15
epsilon_term = 0.0001
first_fix = 1.0 - 0.9**10
second_fix = 1.0 - 0.999**10


def silu_parts(inputs):
    sigmoid_part = jax.nn.sigmoid(inputs)
    silu_slope = sigmoid_part * (1.0 + inputs * (1.0 - sigmoid_part))
    silu_bend = sigmoid_part * (1.0 - sigmoid_part) * (2.0 + inputs * (1.0 - 2.0 * sigmoid_part))
    return (silu_slope, silu_bend)


def adahessian(weight, mean_old, curve_old, gradient, probe_value, product):
    diagonal = probe_value.astype(jnp.float32) * product
    mean_new = first_decay * mean_old + (1.0 - first_decay) * gradient
    curve_new = second_decay * curve_old + (1.0 - second_decay) * diagonal * diagonal
    step_ratio = mean_new / first_fix / (jnp.sqrt(curve_new / second_fix) + epsilon_term)
    weight_new = (weight.astype(jnp.float32) - learn_rate * step_ratio).astype(jnp.bfloat16)
    return (weight_new, mean_new, curve_new)


DP = ("z", "c")
MP = ("x", "y")


def chip_ring(x, n_dp):
    n_chip = n_dp // 2
    d = lax.axis_index(DP)
    z = d // 2
    c = d % 2
    partner = [(i, i ^ 1) for i in range(n_dp)]
    ring = [(2 * j, 2 * ((j + 1) % n_chip)) for j in range(n_chip)] + [
        (2 * j + 1, 2 * ((j - 1) % n_chip) + 1) for j in range(n_chip)
    ]
    px = lax.ppermute(x, DP, partner)
    cur = jnp.concatenate([x, px], 0)
    blocks = [(cur, d, d ^ 1)]
    step = 2 * c - 1
    for k in range(1, n_chip // 2 + 1):
        cur = lax.ppermute(cur, DP, ring)
        j = (z + k * step) % n_chip
        blocks.append((cur, 2 * j + c, 2 * j + 1 - c))
        if k < n_chip // 2:
            ex = lax.ppermute(cur, DP, partner)
            j2 = (z - k * step) % n_chip
            blocks.append((ex, 2 * j2 + 1 - c, 2 * j2 + c))
    return blocks


def step(
    tokens, hidden_grad, gate_weight, up_weight, gate_probe, gate_mean, gate_curve, group_counts
):
    n_dp = lax.axis_size(DP)
    n_mp = lax.axis_size(MP)
    rows_loc, feat = tokens.shape
    shard = feat // n_dp
    width = gate_weight.shape[1]
    d = lax.axis_index(DP)

    t3 = tokens.reshape(rows_loc, n_dp, shard)
    a2a = lax.all_to_all(t3, DP, split_axis=1, concat_axis=1, tiled=True)
    pack = jnp.concatenate([tokens, a2a.reshape(rows_loc, feat)], 0)
    gathered = lax.all_gather(pack, MP, axis=0, tiled=False)
    whole = gathered[:, :rows_loc, :].reshape(n_mp * rows_loc, feat)
    group_rows = whole.shape[0]
    cols = (
        gathered[:, rows_loc:, :]
        .reshape(n_mp, rows_loc, n_dp, shard)
        .transpose(2, 0, 1, 3)
        .reshape(n_dp * group_rows, shard)
    )

    w3 = jnp.concatenate([gate_weight, up_weight, gate_probe], 1)
    blocks = chip_ring(w3, n_dp)
    w_cat = jnp.concatenate([blk for blk, _, _ in blocks], 0)
    part = jnp.concatenate(
        [
            lax.dynamic_slice_in_dim(whole, s * shard, shard, axis=1)
            for _, s0, s1 in blocks
            for s in (s0, s1)
        ],
        1,
    )
    pre = jnp.dot(part, w_cat, preferred_element_type=jnp.float32)
    gate_pre = pre[:, :width]
    up_pre = pre[:, width : 2 * width]
    gate_tan = pre[:, 2 * width :]

    limit = lax.dynamic_index_in_dim(group_counts, d, 0, keepdims=False)
    live = (jnp.arange(group_rows, dtype=jnp.int32) < limit).astype(jnp.float32)
    silu_slope, silu_bend = silu_parts(gate_pre)
    masked = hidden_grad.astype(jnp.float32) * live[:, None]
    grad_gate = (masked * up_pre * silu_slope).astype(jnp.bfloat16)
    tan_gate = (masked * up_pre * silu_bend * gate_tan).astype(jnp.bfloat16)
    packed = jnp.concatenate([grad_gate, tan_gate], 1)

    sums = lax.dot_general(
        cols,
        lax.all_gather(packed, DP, axis=0, tiled=True),
        (((0,), (0,)), ((), ())),
        preferred_element_type=jnp.float32,
    )
    gate_out = adahessian(
        gate_weight, gate_mean, gate_curve, sums[:, :width], gate_probe, sums[:, width:]
    )
    return (gate_out[0], gate_out[1], gate_out[2])


def solution(mesh):
    n_dp, n_mp = mesh.devices.shape
    n_x = len({dev.coords[0] for dev in mesh.devices[0]})
    mesh4 = jax.sharding.Mesh(
        mesh.devices.reshape(n_dp // 2, 2, n_x, n_mp // n_x), ("z", "c", "x", "y")
    )
    every = DP + MP
    return jax.shard_map(
        step,
        mesh=mesh4,
        in_specs=(
            P(every, None),
            P(DP, MP),
            P(DP, MP),
            P(DP, MP),
            P(DP, MP),
            P(DP, MP),
            P(DP, MP),
            P(),
        ),
        out_specs=(P(DP, MP), P(DP, MP), P(DP, MP)),
        check_vma=False,
    )
```

```python
import jax
import jax.numpy as jnp
from jax import lax
from jax.sharding import PartitionSpec as P


first_decay = 0.9
second_decay = 0.999
learn_rate = 0.15
epsilon_term = 0.0001
first_fix = 1.0 - 0.9**10
second_fix = 1.0 - 0.999**10


def silu_parts(inputs):
    sigmoid_part = jax.nn.sigmoid(inputs)
    silu_slope = sigmoid_part * (1.0 + inputs * (1.0 - sigmoid_part))
    silu_bend = sigmoid_part * (1.0 - sigmoid_part) * (2.0 + inputs * (1.0 - 2.0 * sigmoid_part))
    return (silu_slope, silu_bend)


def adahessian(weight, mean_old, curve_old, gradient, probe_value, product):
    diagonal = probe_value.astype(jnp.float32) * product
    mean_new = first_decay * mean_old + (1.0 - first_decay) * gradient
    curve_new = second_decay * curve_old + (1.0 - second_decay) * diagonal * diagonal
    step_ratio = mean_new / first_fix / (jnp.sqrt(curve_new / second_fix) + epsilon_term)
    weight_new = (weight.astype(jnp.float32) - learn_rate * step_ratio).astype(jnp.bfloat16)
    return (weight_new, mean_new, curve_new)


DP = ("z", "c")
MP = ("x", "y")


def chip_ring(x, n_dp):
    n_chip = n_dp // 2
    d = lax.axis_index(DP)
    z = d // 2
    c = d % 2
    partner = [(i, i ^ 1) for i in range(n_dp)]
    ring = [(2 * j, 2 * ((j + 1) % n_chip)) for j in range(n_chip)] + [
        (2 * j + 1, 2 * ((j - 1) % n_chip) + 1) for j in range(n_chip)
    ]
    px = lax.ppermute(x, DP, partner)
    cur = jnp.concatenate([x, px], 0)
    blocks = [(cur, d, d ^ 1)]
    step = 2 * c - 1
    for k in range(1, n_chip // 2 + 1):
        cur = lax.ppermute(cur, DP, ring)
        j = (z + k * step) % n_chip
        blocks.append((cur, 2 * j + c, 2 * j + 1 - c))
        if k < n_chip // 2:
            ex = lax.ppermute(cur, DP, partner)
            j2 = (z - k * step) % n_chip
            blocks.append((ex, 2 * j2 + 1 - c, 2 * j2 + c))
    return blocks


def step(
    tokens, hidden_grad, gate_weight, up_weight, gate_probe, gate_mean, gate_curve, group_counts
):
    n_dp = lax.axis_size(DP)
    n_mp = lax.axis_size(MP)
    rows_loc, feat = tokens.shape
    shard = feat // n_dp
    width = gate_weight.shape[1]
    d = lax.axis_index(DP)

    t3 = tokens.reshape(rows_loc, n_dp, shard)
    a2a = lax.all_to_all(t3, DP, split_axis=1, concat_axis=1, tiled=True)
    pack = jnp.concatenate([tokens, a2a.reshape(rows_loc, feat)], 0)
    gathered = lax.all_gather(pack, MP, axis=0, tiled=False)
    whole = gathered[:, :rows_loc, :].reshape(n_mp * rows_loc, feat)
    group_rows = whole.shape[0]
    cols = (
        gathered[:, rows_loc:, :]
        .reshape(n_mp, rows_loc, n_dp, shard)
        .transpose(2, 0, 1, 3)
        .reshape(n_dp * group_rows, shard)
    )

    w3 = jnp.concatenate([gate_weight, up_weight, gate_probe], 1)
    pre = None
    for block, s0, s1 in chip_ring(w3, n_dp):
        part = jnp.concatenate(
            [
                lax.dynamic_slice_in_dim(whole, s0 * shard, shard, axis=1),
                lax.dynamic_slice_in_dim(whole, s1 * shard, shard, axis=1),
            ],
            1,
        )
        term = jnp.dot(part, block, preferred_element_type=jnp.float32)
        pre = term if pre is None else pre + term
    gate_pre = pre[:, :width]
    up_pre = pre[:, width : 2 * width]
    gate_tan = pre[:, 2 * width :]

    limit = lax.dynamic_index_in_dim(group_counts, d, 0, keepdims=False)
    live = (jnp.arange(group_rows, dtype=jnp.int32) < limit).astype(jnp.float32)
    silu_slope, silu_bend = silu_parts(gate_pre)
    masked = hidden_grad.astype(jnp.float32) * live[:, None]
    grad_gate = (masked * up_pre * silu_slope).astype(jnp.bfloat16)
    tan_gate = (masked * up_pre * silu_bend * gate_tan).astype(jnp.bfloat16)
    packed = jnp.concatenate([grad_gate, tan_gate], 1)

    sums_t = lax.dot_general(
        lax.all_gather(packed, DP, axis=0, tiled=True),
        cols,
        (((0,), (0,)), ((), ())),
        preferred_element_type=jnp.float32,
    )
    gate_out = adahessian(
        gate_weight, gate_mean, gate_curve, sums_t[:width].T, gate_probe, sums_t[width:].T
    )
    return (gate_out[0], gate_out[1], gate_out[2])


def solution(mesh):
    n_dp, n_mp = mesh.devices.shape
    n_x = len({dev.coords[0] for dev in mesh.devices[0]})
    mesh4 = jax.sharding.Mesh(
        mesh.devices.reshape(n_dp // 2, 2, n_x, n_mp // n_x), ("z", "c", "x", "y")
    )
    every = DP + MP
    return jax.shard_map(
        step,
        mesh=mesh4,
        in_specs=(
            P(every, None),
            P(DP, MP),
            P(DP, MP),
            P(DP, MP),
            P(DP, MP),
            P(DP, MP),
            P(DP, MP),
            P(),
        ),
        out_specs=(P(DP, MP), P(DP, MP), P(DP, MP)),
        check_vma=False,
    )
```

```python
import jax
import jax.numpy as jnp
from jax import lax
from jax.sharding import PartitionSpec as P


first_decay = 0.9
second_decay = 0.999
learn_rate = 0.15
epsilon_term = 0.0001
first_fix = 1.0 - 0.9**10
second_fix = 1.0 - 0.999**10


def silu_parts(inputs):
    sigmoid_part = jax.nn.sigmoid(inputs)
    silu_slope = sigmoid_part * (1.0 + inputs * (1.0 - sigmoid_part))
    silu_bend = sigmoid_part * (1.0 - sigmoid_part) * (2.0 + inputs * (1.0 - 2.0 * sigmoid_part))
    return (silu_slope, silu_bend)


def adahessian(weight, mean_old, curve_old, gradient, probe_value, product):
    diagonal = probe_value.astype(jnp.float32) * product
    mean_new = first_decay * mean_old + (1.0 - first_decay) * gradient
    curve_new = second_decay * curve_old + (1.0 - second_decay) * diagonal * diagonal
    step_ratio = mean_new / first_fix / (jnp.sqrt(curve_new / second_fix) + epsilon_term)
    weight_new = (weight.astype(jnp.float32) - learn_rate * step_ratio).astype(jnp.bfloat16)
    return (weight_new, mean_new, curve_new)


DP = ("z", "c")
MP = ("x", "y")


def chip_ring(x, n_dp):
    n_chip = n_dp // 2
    d = lax.axis_index(DP)
    z = d // 2
    c = d % 2
    partner = [(i, i ^ 1) for i in range(n_dp)]
    ring = [(2 * j, 2 * ((j + 1) % n_chip)) for j in range(n_chip)] + [
        (2 * j + 1, 2 * ((j - 1) % n_chip) + 1) for j in range(n_chip)
    ]
    px = lax.ppermute(x, DP, partner)
    cur = jnp.concatenate([x, px], 0)
    blocks = [(cur, d, d ^ 1)]
    step = 2 * c - 1
    for k in range(1, n_chip // 2 + 1):
        cur = lax.ppermute(cur, DP, ring)
        j = (z + k * step) % n_chip
        blocks.append((cur, 2 * j + c, 2 * j + 1 - c))
        if k < n_chip // 2:
            ex = lax.ppermute(cur, DP, partner)
            j2 = (z - k * step) % n_chip
            blocks.append((ex, 2 * j2 + 1 - c, 2 * j2 + c))
    return blocks


def step(
    tokens, hidden_grad, gate_weight, up_weight, gate_probe, gate_mean, gate_curve, group_counts
):
    n_dp = lax.axis_size(DP)
    n_mp = lax.axis_size(MP)
    rows_loc, feat = tokens.shape
    shard = feat // n_dp
    width = gate_weight.shape[1]
    d = lax.axis_index(DP)

    t3 = tokens.reshape(rows_loc, n_dp, shard)
    a2a = lax.all_to_all(t3, DP, split_axis=1, concat_axis=1, tiled=True)
    pack = jnp.concatenate([tokens, a2a.reshape(rows_loc, feat)], 0)
    gathered = lax.all_gather(pack, MP, axis=0, tiled=False)
    whole = gathered[:, :rows_loc, :].reshape(n_mp * rows_loc, feat)
    group_rows = whole.shape[0]
    cols = (
        gathered[:, rows_loc:, :]
        .reshape(n_mp, rows_loc, n_dp, shard)
        .transpose(2, 0, 1, 3)
        .reshape(n_dp * group_rows, shard)
    )

    w3 = jnp.concatenate([gate_weight, up_weight, gate_probe], 1)
    pre = None
    blocks = chip_ring(w3, n_dp)
    for i in range(0, len(blocks), 2):
        pair = jnp.concatenate([blocks[i][0], blocks[i + 1][0]], 0)
        shards = (blocks[i][1], blocks[i][2], blocks[i + 1][1], blocks[i + 1][2])
        part = jnp.concatenate(
            [lax.dynamic_slice_in_dim(whole, s * shard, shard, axis=1) for s in shards], 1
        )
        term = jnp.dot(part, pair, preferred_element_type=jnp.float32)
        pre = term if pre is None else pre + term
    gate_pre = pre[:, :width]
    up_pre = pre[:, width : 2 * width]
    gate_tan = pre[:, 2 * width :]

    limit = lax.dynamic_index_in_dim(group_counts, d, 0, keepdims=False)
    live = (jnp.arange(group_rows, dtype=jnp.int32) < limit).astype(jnp.float32)
    silu_slope, silu_bend = silu_parts(gate_pre)
    masked = hidden_grad.astype(jnp.float32) * live[:, None]
    grad_gate = (masked * up_pre * silu_slope).astype(jnp.bfloat16)
    tan_gate = (masked * up_pre * silu_bend * gate_tan).astype(jnp.bfloat16)
    packed = jnp.concatenate([grad_gate, tan_gate], 1)

    sums_t = lax.dot_general(
        lax.all_gather(packed, DP, axis=0, tiled=True),
        cols,
        (((0,), (0,)), ((), ())),
        preferred_element_type=jnp.float32,
    )
    gate_out = adahessian(
        gate_weight, gate_mean, gate_curve, sums_t[:width].T, gate_probe, sums_t[width:].T
    )
    return (gate_out[0], gate_out[1], gate_out[2])


def solution(mesh):
    n_dp, n_mp = mesh.devices.shape
    n_x = len({dev.coords[0] for dev in mesh.devices[0]})
    mesh4 = jax.sharding.Mesh(
        mesh.devices.reshape(n_dp // 2, 2, n_x, n_mp // n_x), ("z", "c", "x", "y")
    )
    every = DP + MP
    return jax.shard_map(
        step,
        mesh=mesh4,
        in_specs=(
            P(every, None),
            P(DP, MP),
            P(DP, MP),
            P(DP, MP),
            P(DP, MP),
            P(DP, MP),
            P(DP, MP),
            P(),
        ),
        out_specs=(P(DP, MP), P(DP, MP), P(DP, MP)),
        check_vma=False,
    )
```
